32 devices in a mesh: parts: 2 (over y), chain: 4 (over x, core), group: 4 (over z).
Axes of the slice: x: 2, y: 2, z: 4, core: 2. Of those that a mesh axis runs over, the one named last changes fastest.
Arguments:
- rhs: float32 [8, 5, 64, 64], P(('parts', 'chain'), None, None, 'group'), parts along dimension 0, may hold values from -6 to 6
- inv_block: float32 [8, 64, 320, 320], P(('parts', 'chain'), 'group'), parts along dimension 0, may hold values from -0.3125 to 0.3125
- flux_jac: float32 [8, 3, 5, 5, 64], P(('parts', 'chain'), None, None, None, 'group'), parts along dimension 0, may hold values from -2.5 to 2.5
- up_elem: int32 [8, 3, 64], P(('parts', 'chain'), None, 'group'), parts along dimension 0, may hold values from 0 to 63, each once within a row
- lift: float32 [3, 64, 16], replicated, may hold values from -0.875 to 0.875
Outputs:
- solution: float32 [8, 5, 64, 64], P(('parts', 'chain'), None, None, 'group'), parts along dimension 0
The draws below stay inside these ranges and needn't reach their ends.
There are 2 independent parts, one for each index of `parts`. The reference program is written for one: setup_inputs(seed, part) draws one part's arguments, and reference() takes and returns one part's arrays. A program takes and returns all parts, laid end to end along the dimension named above; an argument that names none is the same for every part. Nothing has to cross between parts.
Inputs may be any that keep to these rules, and one draw needn't show every extreme that they name: For every section s and face k, up_elem[s, k, :] names each of the 64 elements once; row s = 0 is not read.
All inputs are finite; a program needn't handle non-finite values.
Results may differ from the reference program's by a relative error of at most 0.02.
Values may be sent and summed in bfloat16 or wider, within the bound.
No kernel may reach another device: no remote copies, remote signals or barrier semaphores. Data moves between devices by JAX's collectives and lax.ppermute only.
A program may use at most 64 MiB of HBM per device.

```python
import jax
import jax.numpy as jnp
from jax import lax

VARS = 5
NP = 4
NODES = 64
FACE = 16
BLOCK = 320
S_TOTAL = 4
E_SECTION = 64


def block_levels(stream_key, shape, cuts, smallest, top_value):
    gain = 1.0
    for axis_at, blocks in cuts:
        draws = jax.random.uniform(jax.random.fold_in(jax.random.fold_in(stream_key, 6), axis_at), (blocks,), jnp.float32, smallest / len(cuts), top_value / len(cuts))
        gain = gain * jnp.repeat(jnp.exp(draws), shape[axis_at] // blocks).reshape((-1,) + (1,) * (len(shape) - 1 - axis_at))
    return gain


def noise(rng, shape, spread, most, split=(), held_as=jnp.bfloat16):
    entries = spread * jax.random.normal(rng, shape, jnp.float32)
    if split:
        entries = entries * block_levels(rng, shape, split, -0.22, 0.18)
    return jnp.clip(entries, -most, most).astype(held_as)


def setup_inputs(seed: int = 0, part: int = 0) -> dict:
    streams_of = jax.random.split(jax.random.key(seed), 6)
    part_splits = jax.random.split(jax.random.fold_in(streams_of[5], part), 6)
    return {
        "rhs": noise(part_splits[0], (S_TOTAL, VARS, NODES, E_SECTION), 1.0, 6.0, ((0, 4), (3, 4)), jnp.float32),
        "inv_block": noise(part_splits[1], (S_TOTAL, E_SECTION, BLOCK, BLOCK), BLOCK ** -0.5, 0.3125, ((0, 4), (1, 4)), jnp.float32),
        "flux_jac": noise(part_splits[2], (S_TOTAL, 3, VARS, VARS, E_SECTION), (VARS + 1) ** -0.5, 2.5, ((0, 4), (4, 4)), jnp.float32),
        "up_elem": jax.vmap(lambda own: jax.random.permutation(own, E_SECTION))(jax.random.split(part_splits[3], S_TOTAL * 3)).reshape((S_TOTAL, 3, E_SECTION)).astype(jnp.int32),
        "lift": noise(streams_of[4], (3, NODES, FACE), (3 * FACE) ** -0.5, 0.875, (), jnp.float32),
    }


HIGH = lax.Precision.HIGHEST


def face_traces(solved):
    elements = solved.shape[-1]
    cube = solved.reshape(VARS, NP, NP, NP, elements)
    first = cube[:, NP - 1, :, :, :].reshape(VARS, FACE, elements)
    second = cube[:, :, NP - 1, :, :].reshape(VARS, FACE, elements)
    third = cube[:, :, :, NP - 1, :].reshape(VARS, FACE, elements)
    return jnp.stack([first, second, third]).astype(jnp.bfloat16)


def solve_section(rhs_s, inv_s, jac_s, up_s, prev_full, lift):
    elements = rhs_s.shape[-1]
    picked = jnp.stack([jnp.take(prev_full[k], up_s[k].astype(jnp.int32), axis=2) for k in range(3)])
    upstream = picked.astype(jnp.float32)
    mixed = jnp.einsum("kwve,kvfe->kwfe", jac_s, upstream, precision=HIGH)
    coupling = jnp.einsum("kif,kwfe->wie", lift, mixed, precision=HIGH)
    flat = (rhs_s - coupling).reshape(VARS * NODES, elements)
    result = jnp.einsum("eij,je->ie", inv_s, flat, precision=HIGH)
    return result.reshape(VARS, NODES, elements)


def reference(rhs, inv_block, flux_jac, up_elem, lift):
    start = jnp.zeros((3, VARS, FACE, E_SECTION), jnp.bfloat16)

    def section_step(prev_full, items):
        rhs_s, inv_s, jac_s, up_s = items
        solved = solve_section(rhs_s, inv_s, jac_s, up_s, prev_full, lift)
        return face_traces(solved), solved

    final, solution = lax.scan(section_step, start, (rhs, inv_block, flux_jac, up_elem))
    return solution
```

```python
import jax
import jax.numpy as jnp
from jax import lax
from jax.sharding import PartitionSpec as P

VARS = 5
NP = 4
NODES = 64
FACE = 16
BLOCK = VARS * NODES

HIGH = lax.Precision.HIGHEST


def face_traces(sol):
    elements = sol.shape[0]
    cube = sol.reshape(elements, VARS, NP, NP, NP)
    first = cube[:, :, NP - 1, :, :].reshape(elements, VARS, FACE)
    second = cube[:, :, :, NP - 1, :].reshape(elements, VARS, FACE)
    third = cube[:, :, :, :, NP - 1].reshape(elements, VARS, FACE)
    return jnp.transpose(jnp.stack([first, second, third]), (0, 2, 3, 1))


def body(rhs, inv_block, flux_jac, up_elem, lift):
    chains = lax.axis_size("chain")
    groups = lax.axis_size("group")
    local = rhs.shape[3]
    c = lax.axis_index("chain")
    g = lax.axis_index("group")

    inv = inv_block[0]
    jac = flux_jac[0]
    up = up_elem[0]
    rhs_t = jnp.transpose(rhs[0], (2, 0, 1)).reshape(local, BLOCK)

    shift = (g - up // local) % groups
    pos = shift * local + up % local
    onehot = (jnp.arange(groups * local)[None, :, None] == pos[:, None, :]).astype(jnp.bfloat16)

    def solve(traces_in):
        if traces_in is None:
            x = rhs_t
        else:
            upstream = jnp.einsum("kvfp,kpe->kvfe", traces_in, onehot, preferred_element_type=jnp.float32)
            mixed = jnp.einsum("kwve,kvfe->kwfe", jac, upstream, precision=HIGH)
            coupling = jnp.einsum("kwfe,kif->ewi", mixed, lift, precision=HIGH)
            x = rhs_t - coupling.reshape(local, BLOCK)
        return jnp.sum(inv * x[:, None, :], axis=-1)

    out = jnp.zeros((local, BLOCK), jnp.float32)
    traces = None
    for turn in range(chains):
        if turn > 0:
            blocks = []
            for d in range(groups):
                pairs = [((turn - 1) * groups + s, turn * groups + (s + d) % groups) for s in range(groups)]
                blocks.append(lax.ppermute(traces, ("chain", "group"), pairs))
            traces_in = jnp.concatenate(blocks, axis=3)
        else:
            traces_in = None
        sol = solve(traces_in)
        out = jnp.where(c == turn, sol, out)
        if turn + 1 < chains:
            traces = face_traces(sol).astype(jnp.bfloat16)
    return jnp.transpose(out.reshape(local, VARS, NODES), (1, 2, 0))[None]


def solution(mesh):
    return jax.shard_map(
        body,
        mesh=mesh,
        in_specs=(
            P(("parts", "chain"), None, None, "group"),
            P(("parts", "chain"), "group", None, None),
            P(("parts", "chain"), None, None, None, "group"),
            P(("parts", "chain"), None, "group"),
            P(),
        ),
        out_specs=P(("parts", "chain"), None, None, "group"),
        check_vma=False,
    )
```

```python
import jax
import jax.numpy as jnp
from jax import lax
from jax.sharding import PartitionSpec as P

VARS = 5
NP = 4
NODES = 64
FACE = 16
BLOCK = VARS * NODES

HIGH = lax.Precision.HIGHEST


def face_traces(sol):
    elements = sol.shape[0]
    cube = sol.reshape(elements, VARS, NP, NP, NP)
    first = cube[:, :, NP - 1, :, :].reshape(elements, VARS, FACE)
    second = cube[:, :, :, NP - 1, :].reshape(elements, VARS, FACE)
    third = cube[:, :, :, :, NP - 1].reshape(elements, VARS, FACE)
    return jnp.transpose(jnp.stack([first, second, third]), (0, 2, 3, 1))


def body(rhs, inv_block, flux_jac, up_elem, lift):
    chains = lax.axis_size("chain")
    groups = lax.axis_size("group")
    local = rhs.shape[3]
    c = lax.axis_index("chain")
    g = lax.axis_index("group")

    inv = inv_block[0]
    jac = flux_jac[0]
    up = up_elem[0]
    rhs_t = jnp.transpose(rhs[0], (2, 0, 1)).reshape(local, BLOCK)

    shift = (g - up // local) % groups
    pos = shift * local + up % local
    onehot = (jnp.arange(groups * local)[None, :, None] == pos[:, None, :]).astype(jnp.bfloat16)

    def coupled(traces_in):
        upstream = jnp.einsum("kvfp,kpe->kvfe", traces_in, onehot, preferred_element_type=jnp.float32)
        mixed = jnp.einsum("kwve,kvfe->kwfe", jac, upstream, precision=HIGH)
        coupling = jnp.einsum("kwfe,kif->ewi", mixed, lift, precision=HIGH)
        return rhs_t - coupling.reshape(local, BLOCK)

    def full_solve(x):
        return jnp.sum(inv * x[:, None, :], axis=-1)

    def trace_rows(x):
        rows = jnp.sum(face_inv * x[:, None, :], axis=-1)
        return jnp.transpose(rows.reshape(local, 3, VARS, FACE), (1, 2, 3, 0))

    def send(traces, turn):
        blocks = []
        for d in range(groups):
            pairs = [((turn - 1) * groups + s, turn * groups + (s + d) % groups) for s in range(groups)]
            blocks.append(lax.ppermute(traces, ("chain", "group"), pairs))
        return jnp.concatenate(blocks, axis=3)

    sol = full_solve(rhs_t)
    out = sol
    traces = face_traces(sol).astype(jnp.bfloat16)
    face_inv = None
    x_prev = None
    for turn in range(1, chains):
        received = send(traces, turn)
        if x_prev is not None:
            out = jnp.where(c == turn - 1, full_solve(x_prev), out)
        if face_inv is None and turn + 1 < chains:
            cube = inv.reshape(local, VARS, NP, NP, NP, BLOCK)
            face_inv = jnp.stack([
                cube[:, :, NP - 1, :, :, :].reshape(local, VARS, FACE, BLOCK),
                cube[:, :, :, NP - 1, :, :].reshape(local, VARS, FACE, BLOCK),
                cube[:, :, :, :, NP - 1, :].reshape(local, VARS, FACE, BLOCK),
            ], axis=1).reshape(local, 3 * VARS * FACE, BLOCK)
        x = coupled(received)
        if turn + 1 < chains:
            traces = trace_rows(x).astype(jnp.bfloat16)
            x_prev = x
        else:
            out = jnp.where(c == turn, full_solve(x), out)
    return jnp.transpose(out.reshape(local, VARS, NODES), (1, 2, 0))[None]


def solution(mesh):
    return jax.shard_map(
        body,
        mesh=mesh,
        in_specs=(
            P(("parts", "chain"), None, None, "group"),
            P(("parts", "chain"), "group", None, None),
            P(("parts", "chain"), None, None, None, "group"),
            P(("parts", "chain"), None, "group"),
            P(),
        ),
        out_specs=P(("parts", "chain"), None, None, "group"),
        check_vma=False,
    )
```

```python
import jax
import jax.numpy as jnp
from jax import lax
from jax.sharding import PartitionSpec as P

VARS = 5
NP = 4
NODES = 64
FACE = 16
BLOCK = VARS * NODES

HIGH = lax.Precision.HIGHEST


def face_traces(sol):
    elements = sol.shape[0]
    cube = sol.reshape(elements, VARS, NP, NP, NP)
    first = cube[:, :, NP - 1, :, :].reshape(elements, VARS, FACE)
    second = cube[:, :, :, NP - 1, :].reshape(elements, VARS, FACE)
    third = cube[:, :, :, :, NP - 1].reshape(elements, VARS, FACE)
    return jnp.transpose(jnp.stack([first, second, third]), (0, 2, 3, 1))


def body(rhs, inv_block, flux_jac, up_elem, lift):
    chains = lax.axis_size("chain")
    groups = lax.axis_size("group")
    local = rhs.shape[3]
    c = lax.axis_index("chain")
    g = lax.axis_index("group")

    inv = inv_block[0]
    jac = flux_jac[0]
    up = up_elem[0]
    rhs_t = jnp.transpose(rhs[0], (2, 0, 1)).reshape(local, BLOCK)

    shift = (g - up // local) % groups
    pos = shift * local + up % local
    onehot = (jnp.arange(groups * local)[None, :, None] == pos[:, None, :]).astype(jnp.bfloat16)

    base = jnp.sum(inv * rhs_t[:, None, :], axis=-1)
    lifted = jnp.einsum("erwi,kif->erwkf", inv.reshape(local, BLOCK, VARS, NODES), lift, precision=HIGH)
    coupled_inv = jnp.einsum("erwkf,kwve->erkvf", lifted, jac, precision=HIGH).reshape(local, BLOCK, 3 * VARS * FACE)

    def solve(traces_in):
        upstream = jnp.einsum("kvfp,kpe->kvfe", traces_in, onehot, preferred_element_type=jnp.float32)
        upstream = jnp.transpose(upstream, (3, 0, 1, 2)).reshape(local, 3 * VARS * FACE)
        return base - jnp.sum(coupled_inv * upstream[:, None, :], axis=-1)

    out = base
    traces = face_traces(base).astype(jnp.bfloat16)
    for turn in range(1, chains):
        blocks = []
        for d in range(groups):
            pairs = [((turn - 1) * groups + s, turn * groups + (s + d) % groups) for s in range(groups)]
            blocks.append(lax.ppermute(traces, ("chain", "group"), pairs))
        sol = solve(jnp.concatenate(blocks, axis=3))
        out = jnp.where(c == turn, sol, out)
        if turn + 1 < chains:
            traces = face_traces(sol).astype(jnp.bfloat16)
    return jnp.transpose(out.reshape(local, VARS, NODES), (1, 2, 0))[None]


def solution(mesh):
    return jax.shard_map(
        body,
        mesh=mesh,
        in_specs=(
            P(("parts", "chain"), None, None, "group"),
            P(("parts", "chain"), "group", None, None),
            P(("parts", "chain"), None, None, None, "group"),
            P(("parts", "chain"), None, "group"),
            P(),
        ),
        out_specs=P(("parts", "chain"), None, None, "group"),
        check_vma=False,
    )
```

```python
import jax
import jax.numpy as jnp
from jax import lax
from jax.sharding import PartitionSpec as P

VARS = 5
NP = 4
NODES = 64
FACE = 16
BLOCK = VARS * NODES

HIGH = lax.Precision.HIGHEST


def face_traces(sol):
    elements = sol.shape[0]
    cube = sol.reshape(elements, VARS, NP, NP, NP)
    first = cube[:, :, NP - 1, :, :].reshape(elements, VARS, FACE)
    second = cube[:, :, :, NP - 1, :].reshape(elements, VARS, FACE)
    third = cube[:, :, :, :, NP - 1].reshape(elements, VARS, FACE)
    return jnp.transpose(jnp.stack([first, second, third]), (0, 2, 3, 1))


def body(rhs, inv_block, flux_jac, up_elem, lift):
    chains = lax.axis_size("chain")
    groups = lax.axis_size("group")
    local = rhs.shape[3]
    c = lax.axis_index("chain")
    g = lax.axis_index("group")

    inv = inv_block[0]
    jac = flux_jac[0]
    up = up_elem[0]
    rhs_t = jnp.transpose(rhs[0], (2, 0, 1)).reshape(local, BLOCK)

    shift = (g - up // local) % groups
    pos = shift * local + up % local
    onehot = (jnp.arange(groups * local)[None, :, None] == pos[:, None, :]).astype(jnp.float32)
    picked_jac = jnp.einsum("kpe,kwve->kvpwe", onehot, jac)

    def solve(traces_in):
        if traces_in is None:
            x = rhs_t
        else:
            mixed = jnp.einsum("kvfp,kvpwe->kwfe", traces_in.astype(jnp.float32), picked_jac, precision=HIGH)
            coupling = jnp.einsum("kwfe,kif->ewi", mixed, lift, precision=HIGH)
            x = rhs_t - coupling.reshape(local, BLOCK)
        return jnp.sum(inv * x[:, None, :], axis=-1)

    out = jnp.zeros((local, BLOCK), jnp.float32)
    traces = None
    for turn in range(chains):
        if turn > 0:
            blocks = []
            for d in range(groups):
                pairs = [((turn - 1) * groups + s, turn * groups + (s + d) % groups) for s in range(groups)]
                blocks.append(lax.ppermute(traces, ("chain", "group"), pairs))
            traces_in = jnp.concatenate(blocks, axis=3)
        else:
            traces_in = None
        sol = solve(traces_in)
        out = jnp.where(c == turn, sol, out)
        if turn + 1 < chains:
            traces = face_traces(sol).astype(jnp.bfloat16)
    return jnp.transpose(out.reshape(local, VARS, NODES), (1, 2, 0))[None]


def solution(mesh):
    return jax.shard_map(
        body,
        mesh=mesh,
        in_specs=(
            P(("parts", "chain"), None, None, "group"),
            P(("parts", "chain"), "group", None, None),
            P(("parts", "chain"), None, None, None, "group"),
            P(("parts", "chain"), None, "group"),
            P(),
        ),
        out_specs=P(("parts", "chain"), None, None, "group"),
        check_vma=False,
    )
```

```python
import jax
import jax.numpy as jnp
from jax import lax
from jax.sharding import PartitionSpec as P

VARS = 5
NP = 4
NODES = 64
FACE = 16
BLOCK = VARS * NODES

HIGH = lax.Precision.HIGHEST


def face_traces(sol):
    elements = sol.shape[0]
    cube = sol.reshape(elements, VARS, NP, NP, NP)
    first = cube[:, :, NP - 1, :, :].reshape(elements, VARS, FACE)
    second = cube[:, :, :, NP - 1, :].reshape(elements, VARS, FACE)
    third = cube[:, :, :, :, NP - 1].reshape(elements, VARS, FACE)
    return jnp.transpose(jnp.stack([first, second, third]), (0, 2, 3, 1))


def body(rhs, inv_block, flux_jac, up_elem, lift):
    chains = lax.axis_size("chain")
    groups = lax.axis_size("group")
    local = rhs.shape[3]
    c = lax.axis_index("chain")
    g = lax.axis_index("group")

    inv = inv_block[0]
    jac = flux_jac[0]
    up = up_elem[0]
    rhs_t = jnp.transpose(rhs[0], (2, 0, 1)).reshape(local, BLOCK)

    shift = (g - up // local) % groups
    pos = shift * local + up % local
    onehot = (jnp.arange(groups * local)[None, :, None] == pos[:, None, :]).astype(jnp.float32)
    picked_jac = jnp.einsum("kpe,kwve->kvpwe", onehot, jac)

    def coupling_of(traces_in):
        mixed = jnp.einsum("kvfp,kvpwe->kwfe", traces_in.astype(jnp.float32), picked_jac, precision=HIGH)
        coupling = jnp.einsum("kwfe,kif->ewi", mixed, lift, precision=HIGH)
        return coupling.reshape(local, BLOCK)

    base = jnp.sum(inv * rhs_t[:, None, :], axis=-1)
    inv_narrow = lax.optimization_barrier(inv.astype(jnp.bfloat16))
    traces = face_traces(base).astype(jnp.bfloat16)
    own_coupling = jnp.zeros((local, BLOCK), jnp.float32)
    for turn in range(1, chains):
        blocks = []
        for d in range(groups):
            pairs = [((turn - 1) * groups + s, turn * groups + (s + d) % groups) for s in range(groups)]
            blocks.append(lax.ppermute(traces, ("chain", "group"), pairs))
        coupling = coupling_of(jnp.concatenate(blocks, axis=3))
        own_coupling = jnp.where(c == turn, coupling, own_coupling)
        if turn + 1 < chains:
            approx = base - jnp.sum(inv_narrow.astype(jnp.float32) * coupling[:, None, :], axis=-1)
            traces = face_traces(approx).astype(jnp.bfloat16)
    out = base - jnp.sum(inv * own_coupling[:, None, :], axis=-1)
    return jnp.transpose(out.reshape(local, VARS, NODES), (1, 2, 0))[None]


def solution(mesh):
    return jax.shard_map(
        body,
        mesh=mesh,
        in_specs=(
            P(("parts", "chain"), None, None, "group"),
            P(("parts", "chain"), "group", None, None),
            P(("parts", "chain"), None, None, None, "group"),
            P(("parts", "chain"), None, "group"),
            P(),
        ),
        out_specs=P(("parts", "chain"), None, None, "group"),
        check_vma=False,
    )
```

```python
import jax
import jax.numpy as jnp
from jax import lax
from jax.sharding import PartitionSpec as P

VARS = 5
NP = 4
NODES = 64
FACE = 16
BLOCK = VARS * NODES

HIGH = lax.Precision.HIGHEST


def face_traces(sol):
    elements = sol.shape[0]
    cube = sol.reshape(elements, VARS, NP, NP, NP)
    first = cube[:, :, NP - 1, :, :].reshape(elements, VARS, FACE)
    second = cube[:, :, :, NP - 1, :].reshape(elements, VARS, FACE)
    third = cube[:, :, :, :, NP - 1].reshape(elements, VARS, FACE)
    return jnp.transpose(jnp.stack([first, second, third]), (0, 2, 3, 1))


def body(rhs, inv_block, flux_jac, up_elem, lift):
    chains = lax.axis_size("chain")
    groups = lax.axis_size("group")
    local = rhs.shape[3]
    c = lax.axis_index("chain")
    g = lax.axis_index("group")

    inv = inv_block[0]
    jac = flux_jac[0]
    up = up_elem[0]
    rhs_t = jnp.transpose(rhs[0], (2, 0, 1)).reshape(local, BLOCK)

    xor_pairs = groups & (groups - 1) == 0
    shift = jnp.bitwise_xor(g, up // local) if xor_pairs else (g - up // local) % groups
    pos = shift * local + up % local
    onehot = (jnp.arange(groups * local)[None, :, None] == pos[:, None, :]).astype(jnp.float32)
    picked_jac = jnp.einsum("kpe,kwve->kvpwe", onehot, jac)

    def solve(traces_in):
        if traces_in is None:
            x = rhs_t
        else:
            mixed = jnp.einsum("kvfp,kvpwe->kwfe", traces_in.astype(jnp.float32), picked_jac, precision=HIGH)
            coupling = jnp.einsum("kwfe,kif->ewi", mixed, lift, precision=HIGH)
            x = rhs_t - coupling.reshape(local, BLOCK)
        return jnp.sum(inv * x[:, None, :], axis=-1)

    out = jnp.zeros((local, BLOCK), jnp.float32)
    traces = None
    for turn in range(chains):
        if turn > 0:
            blocks = [None] * groups
            for d in reversed(range(groups)):
                pairs = [((turn - 1) * groups + s, turn * groups + ((s ^ d) if xor_pairs else (s + d) % groups))
                         for s in range(groups)]
                blocks[d] = lax.ppermute(traces, ("chain", "group"), pairs)
            traces_in = jnp.concatenate(blocks, axis=3)
        else:
            traces_in = None
        sol = solve(traces_in)
        out = jnp.where(c == turn, sol, out)
        if turn + 1 < chains:
            traces = face_traces(sol).astype(jnp.bfloat16)
    return jnp.transpose(out.reshape(local, VARS, NODES), (1, 2, 0))[None]


def solution(mesh):
    return jax.shard_map(
        body,
        mesh=mesh,
        in_specs=(
            P(("parts", "chain"), None, None, "group"),
            P(("parts", "chain"), "group", None, None),
            P(("parts", "chain"), None, None, None, "group"),
            P(("parts", "chain"), None, "group"),
            P(),
        ),
        out_specs=P(("parts", "chain"), None, None, "group"),
        check_vma=False,
    )
```

```python
import jax
import jax.numpy as jnp
from jax import lax
from jax.sharding import PartitionSpec as P

VARS = 5
NP = 4
NODES = 64
FACE = 16
BLOCK = VARS * NODES

HIGH = lax.Precision.HIGHEST


def face_traces(sol):
    elements = sol.shape[0]
    cube = sol.reshape(elements, VARS, NP, NP, NP)
    first = cube[:, :, NP - 1, :, :].reshape(elements, VARS, FACE)
    second = cube[:, :, :, NP - 1, :].reshape(elements, VARS, FACE)
    third = cube[:, :, :, :, NP - 1].reshape(elements, VARS, FACE)
    return jnp.transpose(jnp.stack([first, second, third]), (0, 2, 3, 1))


def body(rhs, inv_block, flux_jac, up_elem, lift):
    chains = lax.axis_size("chain")
    groups = lax.axis_size("group")
    local = rhs.shape[3]
    c = lax.axis_index("chain")
    g = lax.axis_index("group")

    inv = inv_block[0]
    jac = flux_jac[0]
    up = up_elem[0]
    rhs_t = jnp.transpose(rhs[0], (2, 0, 1)).reshape(local, BLOCK)

    xor_pairs = groups & (groups - 1) == 0
    shift = jnp.bitwise_xor(g, up // local) if xor_pairs else (g - up // local) % groups
    pos = shift * local + up % local
    onehot = (jnp.arange(groups * local)[None, :, None] == pos[:, None, :]).astype(jnp.float32)
    picked_jac = jnp.einsum("kpe,kwve->kvpwe", onehot, jac)

    def coupling_of(traces_in):
        mixed = jnp.einsum("kvfp,kvpwe->kwfe", traces_in.astype(jnp.float32), picked_jac, precision=HIGH)
        coupling = jnp.einsum("kwfe,kif->ewi", mixed, lift, precision=HIGH)
        return coupling.reshape(local, BLOCK)

    base = jnp.sum(inv * rhs_t[:, None, :], axis=-1)
    inv_narrow = lax.optimization_barrier(inv.astype(jnp.bfloat16))
    traces = face_traces(base).astype(jnp.bfloat16)
    own_coupling = jnp.zeros((local, BLOCK), jnp.float32)
    for turn in range(1, chains):
        blocks = [None] * groups
        for d in reversed(range(groups)):
            pairs = [((turn - 1) * groups + s, turn * groups + ((s ^ d) if xor_pairs else (s + d) % groups))
                     for s in range(groups)]
            blocks[d] = lax.ppermute(traces, ("chain", "group"), pairs)
        coupling = coupling_of(jnp.concatenate(blocks, axis=3))
        own_coupling = jnp.where(c == turn, coupling, own_coupling)
        if turn + 1 < chains:
            approx = base - jnp.sum(inv_narrow.astype(jnp.float32) * coupling[:, None, :], axis=-1)
            traces = face_traces(approx).astype(jnp.bfloat16)
    out = base - jnp.sum(inv * own_coupling[:, None, :], axis=-1)
    return jnp.transpose(out.reshape(local, VARS, NODES), (1, 2, 0))[None]


def solution(mesh):
    return jax.shard_map(
        body,
        mesh=mesh,
        in_specs=(
            P(("parts", "chain"), None, None, "group"),
            P(("parts", "chain"), "group", None, None),
            P(("parts", "chain"), None, None, None, "group"),
            P(("parts", "chain"), None, "group"),
            P(),
        ),
        out_specs=P(("parts", "chain"), None, None, "group"),
        check_vma=False,
    )
```

```python
import jax
import jax.numpy as jnp
from jax import lax
from jax.sharding import PartitionSpec as P

VARS = 5
NP = 4
NODES = 64
FACE = 16
BLOCK = VARS * NODES

HIGH = lax.Precision.HIGHEST


def face_traces(sol):
    elements = sol.shape[0]
    cube = sol.reshape(elements, VARS, NP, NP, NP)
    first = cube[:, :, NP - 1, :, :].reshape(elements, VARS, FACE)
    second = cube[:, :, :, NP - 1, :].reshape(elements, VARS, FACE)
    third = cube[:, :, :, :, NP - 1].reshape(elements, VARS, FACE)
    return jnp.transpose(jnp.stack([first, second, third]), (0, 2, 3, 1))


def body(rhs, inv_block, flux_jac, up_elem, lift):
    chains = lax.axis_size("chain")
    groups = lax.axis_size("group")
    local = rhs.shape[3]
    c = lax.axis_index("chain")
    g = lax.axis_index("group")

    inv = inv_block[0]
    jac = flux_jac[0]
    up = up_elem[0]
    rhs_t = jnp.transpose(rhs[0], (2, 0, 1)).reshape(local, BLOCK)

    xor_pairs = groups & (groups - 1) == 0
    shift = jnp.bitwise_xor(g, up // local) if xor_pairs else (g - up // local) % groups
    pos = shift * local + up % local
    onehot = (jnp.arange(groups * local)[None, :, None] == pos[:, None, :]).astype(jnp.float32)
    picked_jac = jnp.einsum("kpe,kwve->kvpwe", onehot, jac)

    jac_blocks = [picked_jac[:, :, d * local:(d + 1) * local] for d in range(groups)]

    def coupling_of(blocks):
        mixed = [jnp.einsum("kvfp,kvpwe->kwfe", blocks[d].astype(jnp.float32), jac_blocks[d], precision=HIGH)
                 for d in reversed(range(groups))]
        mixed = sum(mixed[1:], mixed[0])
        coupling = jnp.einsum("kwfe,kif->ewi", mixed, lift, precision=HIGH)
        return coupling.reshape(local, BLOCK)

    base = jnp.sum(inv * rhs_t[:, None, :], axis=-1)
    inv_narrow = lax.optimization_barrier(inv.astype(jnp.bfloat16))
    traces = face_traces(base).astype(jnp.bfloat16)
    own_coupling = jnp.zeros((local, BLOCK), jnp.float32)
    for turn in range(1, chains):
        blocks = [None] * groups
        for d in reversed(range(groups)):
            pairs = [((turn - 1) * groups + s, turn * groups + ((s ^ d) if xor_pairs else (s + d) % groups))
                     for s in range(groups)]
            blocks[d] = lax.ppermute(traces, ("chain", "group"), pairs)
        coupling = coupling_of(blocks)
        own_coupling = jnp.where(c == turn, coupling, own_coupling)
        if turn + 1 < chains:
            approx = base - jnp.sum(inv_narrow.astype(jnp.float32) * coupling[:, None, :], axis=-1)
            traces = face_traces(approx).astype(jnp.bfloat16)
    out = base - jnp.sum(inv * own_coupling[:, None, :], axis=-1)
    return jnp.transpose(out.reshape(local, VARS, NODES), (1, 2, 0))[None]


def solution(mesh):
    return jax.shard_map(
        body,
        mesh=mesh,
        in_specs=(
            P(("parts", "chain"), None, None, "group"),
            P(("parts", "chain"), "group", None, None),
            P(("parts", "chain"), None, None, None, "group"),
            P(("parts", "chain"), None, "group"),
            P(),
        ),
        out_specs=P(("parts", "chain"), None, None, "group"),
        check_vma=False,
    )
```

```python
import jax
import jax.numpy as jnp
from jax import lax
from jax.sharding import PartitionSpec as P

VARS = 5
NP = 4
NODES = 64
FACE = 16
BLOCK = VARS * NODES

HIGH = lax.Precision.HIGHEST


def face_traces(sol):
    elements = sol.shape[0]
    cube = sol.reshape(elements, VARS, NP, NP, NP)
    first = cube[:, :, NP - 1, :, :].reshape(elements, VARS, FACE)
    second = cube[:, :, :, NP - 1, :].reshape(elements, VARS, FACE)
    third = cube[:, :, :, :, NP - 1].reshape(elements, VARS, FACE)
    return jnp.transpose(jnp.stack([first, second, third]), (0, 2, 3, 1))


def body(rhs, inv_block, flux_jac, up_elem, lift):
    chains = lax.axis_size("chain")
    groups = lax.axis_size("group")
    local = rhs.shape[3]
    c = lax.axis_index("chain")
    g = lax.axis_index("group")

    inv = inv_block[0]
    jac = flux_jac[0]
    up = up_elem[0]
    rhs_t = jnp.transpose(rhs[0], (2, 0, 1)).reshape(local, BLOCK)

    xor_pairs = groups & (groups - 1) == 0
    shift = jnp.bitwise_xor(g, up // local) if xor_pairs else (g - up // local) % groups
    pos = shift * local + up % local
    onehot = (jnp.arange(groups * local)[None, :, None] == pos[:, None, :]).astype(jnp.float32)
    picked_jac = jnp.einsum("kpe,kwve->kvpwe", onehot, jac)

    def coupling_of(traces_in):
        mixed = jnp.einsum("kvfp,kvpwe->kwfe", traces_in, picked_jac, precision=HIGH)
        coupling = jnp.einsum("kwfe,kif->ewi", mixed, lift, precision=HIGH)
        return coupling.reshape(local, BLOCK)

    base = jnp.sum(inv * rhs_t[:, None, :], axis=-1)
    inv_narrow = lax.optimization_barrier(inv.astype(jnp.bfloat16))
    traces = face_traces(base)
    own_coupling = jnp.zeros((local, BLOCK), jnp.float32)
    for turn in range(1, chains):
        blocks = [None] * groups
        for d in reversed(range(groups)):
            pairs = [((turn - 1) * groups + s, turn * groups + ((s ^ d) if xor_pairs else (s + d) % groups))
                     for s in range(groups)]
            blocks[d] = lax.ppermute(traces, ("chain", "group"), pairs)
        coupling = coupling_of(jnp.concatenate(blocks, axis=3))
        own_coupling = jnp.where(c == turn, coupling, own_coupling)
        if turn + 1 < chains:
            approx = base - jnp.sum(inv_narrow.astype(jnp.float32) * coupling[:, None, :], axis=-1)
            traces = face_traces(approx)
    out = base - jnp.sum(inv_narrow.astype(jnp.float32) * own_coupling[:, None, :], axis=-1)
    return jnp.transpose(out.reshape(local, VARS, NODES), (1, 2, 0))[None]


def solution(mesh):
    return jax.shard_map(
        body,
        mesh=mesh,
        in_specs=(
            P(("parts", "chain"), None, None, "group"),
            P(("parts", "chain"), "group", None, None),
            P(("parts", "chain"), None, None, None, "group"),
            P(("parts", "chain"), None, "group"),
            P(),
        ),
        out_specs=P(("parts", "chain"), None, None, "group"),
        check_vma=False,
    )
```

```python
import jax
import jax.numpy as jnp
from jax import lax
from jax.sharding import PartitionSpec as P

VARS = 5
NP = 4
NODES = 64
FACE = 16
BLOCK = VARS * NODES

HIGH = lax.Precision.HIGHEST


def face_traces(sol):
    elements = sol.shape[0]
    cube = sol.reshape(elements, VARS, NP, NP, NP)
    first = cube[:, :, NP - 1, :, :].reshape(elements, VARS, FACE)
    second = cube[:, :, :, NP - 1, :].reshape(elements, VARS, FACE)
    third = cube[:, :, :, :, NP - 1].reshape(elements, VARS, FACE)
    return jnp.transpose(jnp.stack([first, second, third]), (0, 2, 3, 1))


def body(rhs, inv_block, flux_jac, up_elem, lift):
    chains = lax.axis_size("chain")
    groups = lax.axis_size("group")
    local = rhs.shape[3]
    c = lax.axis_index("chain")
    g = lax.axis_index("group")

    inv = inv_block[0]
    jac = flux_jac[0]
    up = up_elem[0]
    rhs_t = jnp.transpose(rhs[0], (2, 0, 1)).reshape(local, BLOCK)

    xor_pairs = groups & (groups - 1) == 0
    shift = jnp.bitwise_xor(g, up // local) if xor_pairs else (g - up // local) % groups
    pos = shift * local + up % local
    onehot = (jnp.arange(groups * local)[None, :, None] == pos[:, None, :]).astype(jnp.float32)
    picked_jac = jnp.einsum("kpe,kwve->kvpwe", onehot, jac)

    def coupling_of(traces_in):
        mixed = jnp.einsum("kvfp,kvpwe->kwfe", traces_in.astype(jnp.float32), picked_jac, precision=HIGH)
        coupling = jnp.einsum("kwfe,kif->ewi", mixed, lift, precision=HIGH)
        return coupling.reshape(local, BLOCK)

    base = jnp.sum(inv * rhs_t[:, None, :], axis=-1)
    inv_narrow = lax.optimization_barrier(inv.astype(jnp.bfloat16))
    traces = face_traces(base).astype(jnp.bfloat16)
    own_coupling = jnp.zeros((local, BLOCK), jnp.float32)
    for turn in range(1, chains):
        blocks = [None] * groups
        for d in reversed(range(groups)):
            pairs = [((turn - 1) * groups + s, turn * groups + ((s ^ d) if xor_pairs else (s + d) % groups))
                     for s in range(groups)]
            blocks[d] = lax.ppermute(traces, ("chain", "group"), pairs)
        coupling = coupling_of(jnp.concatenate(blocks, axis=3))
        own_coupling = jnp.where(c == turn, coupling, own_coupling)
        if turn + 1 < chains:
            approx = base - jnp.sum(inv_narrow.astype(jnp.float32) * coupling[:, None, :], axis=-1)
            traces = face_traces(approx).astype(jnp.bfloat16)
    out = base - jnp.sum(inv_narrow.astype(jnp.float32) * own_coupling[:, None, :], axis=-1)
    return jnp.transpose(out.reshape(local, VARS, NODES), (1, 2, 0))[None]


def solution(mesh):
    return jax.shard_map(
        body,
        mesh=mesh,
        in_specs=(
            P(("parts", "chain"), None, None, "group"),
            P(("parts", "chain"), "group", None, None),
            P(("parts", "chain"), None, None, None, "group"),
            P(("parts", "chain"), None, "group"),
            P(),
        ),
        out_specs=P(("parts", "chain"), None, None, "group"),
        check_vma=False,
    )
```

```python
import jax
import jax.numpy as jnp
from jax import lax
from jax.sharding import PartitionSpec as P

VARS = 5
NP = 4
NODES = 64
FACE = 16
BLOCK = VARS * NODES

HIGH = lax.Precision.HIGHEST
HIGHEST = lax.Precision.HIGHEST


def face_traces(sol):
    elements = sol.shape[0]
    cube = sol.reshape(elements, VARS, NP, NP, NP)
    first = cube[:, :, NP - 1, :, :].reshape(elements, VARS, FACE)
    second = cube[:, :, :, NP - 1, :].reshape(elements, VARS, FACE)
    third = cube[:, :, :, :, NP - 1].reshape(elements, VARS, FACE)
    return jnp.transpose(jnp.stack([first, second, third]), (0, 2, 3, 1))


def body(rhs, inv_block, flux_jac, up_elem, lift):
    chains = lax.axis_size("chain")
    groups = lax.axis_size("group")
    local = rhs.shape[3]
    c = lax.axis_index("chain")
    g = lax.axis_index("group")

    inv = inv_block[0]
    jac = flux_jac[0]
    up = up_elem[0]
    rhs_t = jnp.transpose(rhs[0], (2, 0, 1)).reshape(local, BLOCK)
    eye = jnp.eye(local, dtype=jnp.float32)

    xor_pairs = groups & (groups - 1) == 0
    shift = jnp.bitwise_xor(g, up // local) if xor_pairs else (g - up // local) % groups
    pos = shift * local + up % local
    onehot = (jnp.arange(groups * local)[None, :, None] == pos[:, None, :]).astype(jnp.float32)
    picked_jac = jnp.einsum("kpe,kwve->kvpwe", onehot, jac)

    def coupling_of(traces_in):
        mixed = jnp.einsum("kvfp,kvpwe->kwfe", traces_in.astype(jnp.float32), picked_jac, precision=HIGH)
        coupling = jnp.einsum("kwfe,kif->ewi", mixed, lift, precision=HIGH)
        return coupling.reshape(local, BLOCK)

    base = jnp.sum(inv * rhs_t[:, None, :], axis=-1)
    inv_narrow = lax.optimization_barrier(inv.astype(jnp.bfloat16))
    traces = face_traces(base).astype(jnp.bfloat16)
    own_coupling = jnp.zeros((local, BLOCK), jnp.float32)
    for turn in range(1, chains):
        blocks = [None] * groups
        for d in reversed(range(groups)):
            pairs = [((turn - 1) * groups + s, turn * groups + ((s ^ d) if xor_pairs else (s + d) % groups))
                     for s in range(groups)]
            blocks[d] = lax.ppermute(traces, ("chain", "group"), pairs)
        coupling = coupling_of(jnp.concatenate(blocks, axis=3))
        own_coupling = jnp.where(c == turn, coupling, own_coupling)
        if turn + 1 < chains:
            approx = base - jnp.sum(inv_narrow.astype(jnp.float32) * coupling[:, None, :], axis=-1)
            traces = face_traces(approx).astype(jnp.bfloat16)
    out = base - jnp.sum(inv_narrow.astype(jnp.float32) * own_coupling[:, None, :], axis=-1)
    out = jnp.einsum("evi,ef->vfi", out.reshape(local, VARS, NODES), eye, precision=HIGHEST)
    return jnp.transpose(out, (0, 2, 1))[None]


def solution(mesh):
    return jax.shard_map(
        body,
        mesh=mesh,
        in_specs=(
            P(("parts", "chain"), None, None, "group"),
            P(("parts", "chain"), "group", None, None),
            P(("parts", "chain"), None, None, None, "group"),
            P(("parts", "chain"), None, "group"),
            P(),
        ),
        out_specs=P(("parts", "chain"), None, None, "group"),
        check_vma=False,
    )
```

```python
import jax
import numpy as np
import jax.numpy as jnp
from jax import lax
from jax.sharding import PartitionSpec as P

VARS = 5
NP = 4
NODES = 64
FACE = 16
BLOCK = VARS * NODES

HIGH = lax.Precision.HIGHEST


def face_traces(sol):
    elements = sol.shape[0]
    cube = sol.reshape(elements, VARS, NP, NP, NP)
    first = cube[:, :, NP - 1, :, :].reshape(elements, VARS, FACE)
    second = cube[:, :, :, NP - 1, :].reshape(elements, VARS, FACE)
    third = cube[:, :, :, :, NP - 1].reshape(elements, VARS, FACE)
    return jnp.transpose(jnp.stack([first, second, third]), (0, 2, 3, 1))


def body(rhs, inv_block, flux_jac, up_elem, lift):
    chains = lax.axis_size("chain")
    groups = lax.axis_size("group")
    local = rhs.shape[3]
    c = lax.axis_index("chain")
    g = lax.axis_index("group")

    inv = inv_block[0]
    jac = flux_jac[0]
    up = up_elem[0]
    rhs_t = jnp.transpose(rhs[0], (2, 0, 1)).reshape(local, BLOCK)

    xor_pairs = groups & (groups - 1) == 0
    shift = jnp.bitwise_xor(g, up // local) if xor_pairs else (g - up // local) % groups
    pos = shift * local + up % local
    onehot = (jnp.arange(groups * local)[None, :, None] == pos[:, None, :]).astype(jnp.float32)
    picked_jac = jnp.einsum("kpe,kwve->kvpwe", onehot, jac)

    def coupling_of(traces_in):
        mixed = jnp.einsum("kvfp,kvpwe->kwfe", traces_in.astype(jnp.float32), picked_jac, precision=HIGH)
        coupling = jnp.einsum("kwfe,kif->ewi", mixed, lift, precision=HIGH)
        return coupling.reshape(local, BLOCK)

    base = jnp.sum(inv * rhs_t[:, None, :], axis=-1)
    inv_narrow = lax.optimization_barrier(inv.astype(jnp.bfloat16))
    f = np.arange(FACE)
    face_nodes = np.stack([48 + f, (f // 4) * 16 + 12 + f % 4, (f // 4) * 16 + (f % 4) * 4 + 3])
    face_rows = (np.arange(VARS)[None, :, None] * NODES + face_nodes[:, None, :]).reshape(-1)
    face_inv = lax.optimization_barrier(jnp.take(inv, face_rows, axis=1).astype(jnp.bfloat16))
    face_base = jnp.take(base, face_rows, axis=1)
    traces = face_traces(base).astype(jnp.bfloat16)
    own_coupling = jnp.zeros((local, BLOCK), jnp.float32)
    for turn in range(1, chains):
        blocks = [None] * groups
        for d in reversed(range(groups)):
            pairs = [((turn - 1) * groups + s, turn * groups + ((s ^ d) if xor_pairs else (s + d) % groups))
                     for s in range(groups)]
            blocks[d] = lax.ppermute(traces, ("chain", "group"), pairs)
        coupling = coupling_of(jnp.concatenate(blocks, axis=3))
        own_coupling = jnp.where(c == turn, coupling, own_coupling)
        if turn + 1 < chains:
            approx = face_base - jnp.sum(face_inv.astype(jnp.float32) * coupling[:, None, :], axis=-1)
            traces = jnp.transpose(approx.reshape(local, 3, VARS, FACE), (1, 2, 3, 0)).astype(jnp.bfloat16)
    out = base - jnp.sum(inv_narrow.astype(jnp.float32) * own_coupling[:, None, :], axis=-1)
    return jnp.transpose(out.reshape(local, VARS, NODES), (1, 2, 0))[None]


def solution(mesh):
    return jax.shard_map(
        body,
        mesh=mesh,
        in_specs=(
            P(("parts", "chain"), None, None, "group"),
            P(("parts", "chain"), "group", None, None),
            P(("parts", "chain"), None, None, None, "group"),
            P(("parts", "chain"), None, "group"),
            P(),
        ),
        out_specs=P(("parts", "chain"), None, None, "group"),
        check_vma=False,
    )
```

```python
import jax
import jax.numpy as jnp
from jax import lax
from jax.sharding import PartitionSpec as P

VARS = 5
NP = 4
NODES = 64
FACE = 16
BLOCK = VARS * NODES

HIGH = lax.Precision.HIGHEST


def face_traces(sol):
    elements = sol.shape[0]
    cube = sol.reshape(elements, VARS, NP, NP, NP)
    first = cube[:, :, NP - 1, :, :].reshape(elements, VARS, FACE)
    second = cube[:, :, :, NP - 1, :].reshape(elements, VARS, FACE)
    third = cube[:, :, :, :, NP - 1].reshape(elements, VARS, FACE)
    return jnp.transpose(jnp.stack([first, second, third]), (0, 2, 3, 1))


def body(rhs, inv_block, flux_jac, up_elem, lift):
    chains = lax.axis_size("chain")
    groups = lax.axis_size("group")
    local = rhs.shape[3]
    c = lax.axis_index("chain")
    g = lax.axis_index("group")

    inv = inv_block[0]
    jac = flux_jac[0]
    up = up_elem[0]
    rhs_t = jnp.transpose(rhs[0], (2, 0, 1)).reshape(local, BLOCK)

    xor_pairs = groups & (groups - 1) == 0
    shift = jnp.bitwise_xor(g, up // local) if xor_pairs else (g - up // local) % groups
    pos = shift * local + up % local
    onehot = (jnp.arange(groups * local)[None, :, None] == pos[:, None, :]).astype(jnp.float32)
    picked_jac = jnp.einsum("kpe,kwve->kvpwe", onehot, jac)

    def coupling_of(traces_in):
        mixed = jnp.einsum("kvfp,kvpwe->kwfe", traces_in.astype(jnp.float32), picked_jac, precision=HIGH)
        coupling = jnp.einsum("kwfe,kif->ewi", mixed, lift, precision=HIGH)
        return coupling.reshape(local, BLOCK)

    base = jnp.sum(inv * rhs_t[:, None, :], axis=-1)
    inv_narrow = lax.optimization_barrier(
        jnp.transpose(inv, (1, 0, 2)).astype(jnp.bfloat16).reshape(BLOCK * local, BLOCK))

    def narrow_solve(x):
        rows = inv_narrow.reshape(BLOCK, local, BLOCK).astype(jnp.float32)
        return jnp.transpose(jnp.sum(rows * x[None, :, :], axis=-1))
    traces = face_traces(base).astype(jnp.bfloat16)
    own_coupling = jnp.zeros((local, BLOCK), jnp.float32)
    for turn in range(1, chains):
        blocks = [None] * groups
        for d in reversed(range(groups)):
            pairs = [((turn - 1) * groups + s, turn * groups + ((s ^ d) if xor_pairs else (s + d) % groups))
                     for s in range(groups)]
            blocks[d] = lax.ppermute(traces, ("chain", "group"), pairs)
        coupling = coupling_of(jnp.concatenate(blocks, axis=3))
        own_coupling = jnp.where(c == turn, coupling, own_coupling)
        if turn + 1 < chains:
            approx = base - narrow_solve(coupling)
            traces = face_traces(approx).astype(jnp.bfloat16)
    out = base - narrow_solve(own_coupling)
    return jnp.transpose(out.reshape(local, VARS, NODES), (1, 2, 0))[None]


def solution(mesh):
    return jax.shard_map(
        body,
        mesh=mesh,
        in_specs=(
            P(("parts", "chain"), None, None, "group"),
            P(("parts", "chain"), "group", None, None),
            P(("parts", "chain"), None, None, None, "group"),
            P(("parts", "chain"), None, "group"),
            P(),
        ),
        out_specs=P(("parts", "chain"), None, None, "group"),
        check_vma=False,
    )
```

```python
import jax
import numpy as np
import jax.numpy as jnp
from jax import lax
from jax.sharding import PartitionSpec as P

VARS = 5
NP = 4
NODES = 64
FACE = 16
BLOCK = VARS * NODES

HIGH = lax.Precision.HIGHEST


def face_traces(sol):
    elements = sol.shape[0]
    cube = sol.reshape(elements, VARS, NP, NP, NP)
    first = cube[:, :, NP - 1, :, :].reshape(elements, VARS, FACE)
    second = cube[:, :, :, NP - 1, :].reshape(elements, VARS, FACE)
    third = cube[:, :, :, :, NP - 1].reshape(elements, VARS, FACE)
    return jnp.transpose(jnp.stack([first, second, third]), (0, 2, 3, 1))


def body(rhs, inv_block, flux_jac, up_elem, lift):
    chains = lax.axis_size("chain")
    groups = lax.axis_size("group")
    local = rhs.shape[3]
    c = lax.axis_index("chain")
    g = lax.axis_index("group")

    inv = inv_block[0]
    jac = flux_jac[0]
    up = up_elem[0]
    rhs_t = jnp.transpose(rhs[0], (2, 0, 1)).reshape(local, BLOCK)

    xor_pairs = groups & (groups - 1) == 0
    shift = jnp.bitwise_xor(g, up // local) if xor_pairs else (g - up // local) % groups
    pos = shift * local + up % local
    onehot = (jnp.arange(groups * local)[None, :, None] == pos[:, None, :]).astype(jnp.float32)
    picked_jac = jnp.einsum("kpe,kwve->kvpwe", onehot, jac)

    def coupling_of(traces_in):
        mixed = jnp.einsum("kvfp,kvpwe->kwfe", traces_in.astype(jnp.float32), picked_jac, precision=HIGH)
        coupling = jnp.einsum("kwfe,kif->ewi", mixed, lift, precision=HIGH)
        return coupling.reshape(local, BLOCK)

    base = jnp.sum(inv * rhs_t[:, None, :], axis=-1)
    inv_narrow = lax.optimization_barrier(inv.astype(jnp.bfloat16))
    traces = face_traces(base).astype(jnp.bfloat16)
    own_coupling = jnp.zeros((local, BLOCK), jnp.float32)
    f = np.arange(FACE)
    face_nodes = np.stack([48 + f, (f // 4) * 16 + 12 + f % 4, (f // 4) * 16 + (f % 4) * 4 + 3])
    face_rows = (np.arange(VARS)[None, :, None] * NODES + face_nodes[:, None, :]).reshape(-1)
    face_base = jnp.transpose(face_traces(base), (3, 0, 1, 2)).reshape(local, 3 * VARS * FACE)
    face_inv = None
    for turn in range(1, chains):
        if face_inv is None and turn >= 2 and turn + 1 < chains:
            narrow_now, _ = lax.optimization_barrier((inv_narrow, traces))
            face_inv = lax.optimization_barrier(jnp.take(narrow_now, face_rows, axis=1))
        blocks = [None] * groups
        for d in reversed(range(groups)):
            pairs = [((turn - 1) * groups + s, turn * groups + ((s ^ d) if xor_pairs else (s + d) % groups))
                     for s in range(groups)]
            blocks[d] = lax.ppermute(traces, ("chain", "group"), pairs)
        coupling = coupling_of(jnp.concatenate(blocks, axis=3))
        own_coupling = jnp.where(c == turn, coupling, own_coupling)
        if turn + 1 < chains:
            if face_inv is None:
                approx = base - jnp.sum(inv_narrow.astype(jnp.float32) * coupling[:, None, :], axis=-1)
                traces = face_traces(approx).astype(jnp.bfloat16)
            else:
                approx = face_base - jnp.sum(face_inv.astype(jnp.float32) * coupling[:, None, :], axis=-1)
                traces = jnp.transpose(approx.reshape(local, 3, VARS, FACE), (1, 2, 3, 0)).astype(jnp.bfloat16)
    out = base - jnp.sum(inv_narrow.astype(jnp.float32) * own_coupling[:, None, :], axis=-1)
    return jnp.transpose(out.reshape(local, VARS, NODES), (1, 2, 0))[None]


def solution(mesh):
    return jax.shard_map(
        body,
        mesh=mesh,
        in_specs=(
            P(("parts", "chain"), None, None, "group"),
            P(("parts", "chain"), "group", None, None),
            P(("parts", "chain"), None, None, None, "group"),
            P(("parts", "chain"), None, "group"),
            P(),
        ),
        out_specs=P(("parts", "chain"), None, None, "group"),
        check_vma=False,
    )
```

```python
import jax
import jax.numpy as jnp
from jax import lax
from jax.sharding import PartitionSpec as P

VARS = 5
NP = 4
NODES = 64
FACE = 16
BLOCK = VARS * NODES

HIGH = lax.Precision.HIGHEST


def face_traces(sol):
    elements = sol.shape[0]
    cube = sol.reshape(elements, VARS, NP, NP, NP)
    first = cube[:, :, NP - 1, :, :].reshape(elements, VARS, FACE)
    second = cube[:, :, :, NP - 1, :].reshape(elements, VARS, FACE)
    third = cube[:, :, :, :, NP - 1].reshape(elements, VARS, FACE)
    return jnp.transpose(jnp.stack([first, second, third]), (0, 2, 3, 1))


def body(rhs, inv_block, flux_jac, up_elem, lift):
    chains = lax.axis_size("chain")
    groups = lax.axis_size("group")
    local = rhs.shape[3]
    c = lax.axis_index("chain")
    g = lax.axis_index("group")

    inv = inv_block[0]
    jac = flux_jac[0]
    up = up_elem[0]
    rhs_t = jnp.transpose(rhs[0], (2, 0, 1)).reshape(local, BLOCK)

    xor_pairs = groups & (groups - 1) == 0
    shift = jnp.bitwise_xor(g, up // local) if xor_pairs else (g - up // local) % groups
    pos = shift * local + up % local
    onehot = (jnp.arange(groups * local)[None, :, None] == pos[:, None, :]).astype(jnp.float32)
    picked_jac = jnp.einsum("kpe,kwve->kvpwe", onehot, jac)

    def coupling_of(traces_in):
        mixed = jnp.einsum("kvfp,kvpwe->kwfe", traces_in.astype(jnp.float32), picked_jac, precision=lax.Precision.HIGH)
        coupling = jnp.einsum("kwfe,kif->ewi", mixed, lift, precision=lax.Precision.HIGH)
        return coupling.reshape(local, BLOCK)

    base = jnp.sum(inv * rhs_t[:, None, :], axis=-1)
    inv_narrow = lax.optimization_barrier(inv.astype(jnp.bfloat16))
    traces = face_traces(base).astype(jnp.bfloat16)
    own_coupling = jnp.zeros((local, BLOCK), jnp.float32)
    for turn in range(1, chains):
        blocks = [None] * groups
        for d in reversed(range(groups)):
            pairs = [((turn - 1) * groups + s, turn * groups + ((s ^ d) if xor_pairs else (s + d) % groups))
                     for s in range(groups)]
            blocks[d] = lax.ppermute(traces, ("chain", "group"), pairs)
        coupling = coupling_of(jnp.concatenate(blocks, axis=3))
        own_coupling = jnp.where(c == turn, coupling, own_coupling)
        if turn + 1 < chains:
            approx = base - jnp.sum(inv_narrow.astype(jnp.float32) * coupling[:, None, :], axis=-1)
            traces = face_traces(approx).astype(jnp.bfloat16)
    out = base - jnp.sum(inv_narrow.astype(jnp.float32) * own_coupling[:, None, :], axis=-1)
    return jnp.transpose(out.reshape(local, VARS, NODES), (1, 2, 0))[None]


def solution(mesh):
    return jax.shard_map(
        body,
        mesh=mesh,
        in_specs=(
            P(("parts", "chain"), None, None, "group"),
            P(("parts", "chain"), "group", None, None),
            P(("parts", "chain"), None, None, None, "group"),
            P(("parts", "chain"), None, "group"),
            P(),
        ),
        out_specs=P(("parts", "chain"), None, None, "group"),
        check_vma=False,
    )
```

```python
import jax
import jax.numpy as jnp
from jax import lax
from jax.sharding import PartitionSpec as P

VARS = 5
NP = 4
NODES = 64
FACE = 16
BLOCK = VARS * NODES

HIGH = lax.Precision.HIGHEST


def face_traces(sol):
    elements = sol.shape[0]
    cube = sol.reshape(elements, VARS, NP, NP, NP)
    first = cube[:, :, NP - 1, :, :].reshape(elements, VARS, FACE)
    second = cube[:, :, :, NP - 1, :].reshape(elements, VARS, FACE)
    third = cube[:, :, :, :, NP - 1].reshape(elements, VARS, FACE)
    return jnp.transpose(jnp.stack([first, second, third]), (0, 2, 3, 1))


def body(rhs, inv_block, flux_jac, up_elem, lift):
    chains = lax.axis_size("chain")
    groups = lax.axis_size("group")
    local = rhs.shape[3]
    c = lax.axis_index("chain")
    g = lax.axis_index("group")

    inv = inv_block[0]
    jac = flux_jac[0]
    up = up_elem[0]
    rhs_t = jnp.transpose(rhs[0], (2, 0, 1)).reshape(local, BLOCK)

    xor_pairs = groups & (groups - 1) == 0
    shift = jnp.bitwise_xor(g, up // local) if xor_pairs else (g - up // local) % groups
    pos = shift * local + up % local
    onehot = (jnp.arange(groups * local)[None, :, None] == pos[:, None, :]).astype(jnp.float32)
    picked_jac = jnp.einsum("kpe,kwve->kvpwe", onehot, jac)
    jac_high = picked_jac.astype(jnp.bfloat16).astype(jnp.float32)
    jac_low = (picked_jac - jac_high).astype(jnp.bfloat16).astype(jnp.float32)
    jac_split = jnp.concatenate([jac_high, jac_low], axis=2)

    def coupling_of(traces_in):
        doubled = jnp.concatenate([traces_in, traces_in], axis=3).astype(jnp.float32)
        mixed = jnp.einsum("kvfp,kvpwe->kwfe", doubled, jac_split, precision=lax.Precision.DEFAULT)
        coupling = jnp.einsum("kwfe,kif->ewi", mixed, lift, precision=lax.Precision.HIGH)
        return coupling.reshape(local, BLOCK)

    base = jnp.sum(inv * rhs_t[:, None, :], axis=-1)
    inv_narrow = lax.optimization_barrier(inv.astype(jnp.bfloat16))
    traces = face_traces(base).astype(jnp.bfloat16)
    own_coupling = jnp.zeros((local, BLOCK), jnp.float32)
    for turn in range(1, chains):
        blocks = [None] * groups
        for d in reversed(range(groups)):
            pairs = [((turn - 1) * groups + s, turn * groups + ((s ^ d) if xor_pairs else (s + d) % groups))
                     for s in range(groups)]
            blocks[d] = lax.ppermute(traces, ("chain", "group"), pairs)
        coupling = coupling_of(jnp.concatenate(blocks, axis=3))
        own_coupling = jnp.where(c == turn, coupling, own_coupling)
        if turn + 1 < chains:
            approx = base - jnp.sum(inv_narrow.astype(jnp.float32) * coupling[:, None, :], axis=-1)
            traces = face_traces(approx).astype(jnp.bfloat16)
    out = base - jnp.sum(inv_narrow.astype(jnp.float32) * own_coupling[:, None, :], axis=-1)
    return jnp.transpose(out.reshape(local, VARS, NODES), (1, 2, 0))[None]


def solution(mesh):
    return jax.shard_map(
        body,
        mesh=mesh,
        in_specs=(
            P(("parts", "chain"), None, None, "group"),
            P(("parts", "chain"), "group", None, None),
            P(("parts", "chain"), None, None, None, "group"),
            P(("parts", "chain"), None, "group"),
            P(),
        ),
        out_specs=P(("parts", "chain"), None, None, "group"),
        check_vma=False,
    )
```
